768 devices in a mesh: group: 16 (over y, core), frame: 48 (over x, z).
Axes of the slice: x: 4, y: 8, z: 12, core: 2. Of those that a mesh axis runs over, the one named last changes fastest.
Arguments:
- video: bfloat16 [48, 48, 128, 384], P('group', 'frame'), may hold values from -6 to 6
- kernel3: bfloat16 [3, 3, 3, 384, 384], replicated, may hold values from -0.0625 to 0.0625
- kernel2: bfloat16 [3, 3, 384, 384], replicated, may hold values from -0.109375 to 0.109375
Outputs:
- features: bfloat16 [48, 48, 128, 384], P('group', 'frame')
- critic: bfloat16 [48, 48, 128, 384], P('frame', None, 'group')
The draws below stay inside these ranges and needn't reach their ends.
All inputs are finite; a program needn't handle non-finite values.
Results may differ from the reference program's by a relative error of at most 0.005.
Values may be sent and summed in bfloat16 or wider, within the bound.
No kernel may reach another device: no remote copies, remote signals or barrier semaphores. Data moves between devices by JAX's collectives and lax.ppermute only.
A program may use at most 64 MiB of HBM per device.

```python
import jax
import jax.numpy as jnp
from jax import lax

C = 384
W = 128
TF = 48
H = 48


def levels(own_key, shape, shards, low, largest):
    level, own = 1.0, jax.random.fold_in(own_key, 6)
    for dim, blocks in shards:
        steps = jnp.exp(jax.random.uniform(jax.random.fold_in(own, dim), (blocks,), jnp.float32, low / len(shards), largest / len(shards)))
        level = level * jnp.repeat(steps, shape[dim] // blocks).reshape([-1 if axis == dim else 1 for axis in range(len(shape))])
    return level


def normal_values(stream_key, dims, width, reach, cuts=(), kind=jnp.bfloat16):
    values = jax.random.normal(stream_key, dims, jnp.float32) * width
    if len(cuts) > 0:
        values = levels(stream_key, dims, cuts, -0.22, 0.18) * values
    return jnp.clip(values, min=-reach, max=reach).astype(kind)


def setup_inputs(seed: int = 0) -> dict:
    streams_of = jax.random.split(jax.random.key(seed), 4)
    return {
        "video": normal_values(streams_of[0], (TF, H, W, C), 1.0, 6.0, ((0, 16), (1, 48))),
        "kernel3": normal_values(streams_of[1], (3, 3, 3, C, C), (27 * C) ** -0.5, 0.0625),
        "kernel2": normal_values(streams_of[2], (3, 3, C, C), (9 * C) ** -0.5, 0.109375),
    }


def reference(video, kernel3, kernel2):
    source = video.astype(jnp.float32)[None]
    conv = lax.conv_general_dilated(source, kernel3.astype(jnp.float32), (1, 1, 1), ((2, 0), (1, 1), (1, 1)), dimension_numbers=("NDHWC", "DHWIO", "NDHWC"), preferred_element_type=jnp.float32)[0]
    features = jax.nn.silu(conv).astype(jnp.bfloat16)
    critic = lax.conv_general_dilated(features.astype(jnp.float32), kernel2.astype(jnp.float32), (1, 1), ((1, 1), (1, 1)), dimension_numbers=("NHWC", "HWIO", "NHWC"), preferred_element_type=jnp.float32)
    return features, critic.astype(jnp.bfloat16)
```

```python
import jax
import jax.numpy as jnp
from jax import lax
from jax.sharding import PartitionSpec as P


def shifted(value, axis, steps):
    count = lax.axis_size(axis)
    first, last = (max(0, -steps), min(count, count - steps))
    return lax.ppermute(value, axis, [(source, source + steps) for source in range(first, last)])


def diagonal(value, group_steps, frame_steps):
    groups, frames = lax.axis_size("group"), lax.axis_size("frame")
    pairs = []
    for g in range(groups):
        for f in range(frames):
            h, e = g + group_steps, f + frame_steps
            if 0 <= h < groups and 0 <= e < frames:
                pairs.append((g * frames + f, h * frames + e))
    return lax.ppermute(value, ("group", "frame"), pairs)


def conv3d(rows, kernel3):
    return lax.conv_general_dilated(
        rows[None],
        kernel3,
        (1, 1, 1),
        ((0, 0), (0, 0), (1, 1)),
        dimension_numbers=("NDHWC", "DHWIO", "NDHWC"),
        preferred_element_type=jnp.float32,
    )[0, :, 0]


def shards(video, kernel3, kernel2):
    length, _, width, channels = video.shape
    groups = lax.axis_size("group")
    cached = shifted(video[length - 2 :], "group", 1)
    above = shifted(video, "frame", 1)
    below = shifted(video, "frame", -1)
    cached_above = diagonal(video[length - 2 :], 1, 1)
    cached_below = diagonal(video[length - 2 :], 1, -1)
    rows = jnp.concatenate(
        [
            jnp.concatenate([cached_above, above], 0),
            jnp.concatenate([cached, video], 0),
            jnp.concatenate([cached_below, below], 0),
        ],
        1,
    )
    conv = conv3d(rows, kernel3)
    features = jax.nn.silu(conv).astype(jnp.bfloat16)
    block = width // groups
    padded = jnp.pad(features, ((0, 0), (1, 1), (0, 0)))
    pieces = jnp.stack([padded[:, j * block : j * block + block + 2] for j in range(groups)], 0)
    pieces = lax.all_to_all(pieces, "group", 0, 0, tiled=False)
    pieces = pieces.reshape(groups * length, block + 2, channels)
    rows_all = lax.all_to_all(pieces, "frame", 0, 0, tiled=True)
    critic = lax.conv_general_dilated(
        rows_all[None],
        kernel2,
        (1, 1),
        ((1, 1), (0, 0)),
        dimension_numbers=("NHWC", "HWIO", "NHWC"),
        preferred_element_type=jnp.float32,
    ).astype(jnp.bfloat16)
    return features[:, None], critic


def solution(mesh):
    return jax.shard_map(
        shards,
        mesh=mesh,
        in_specs=(P("group", "frame", None, None), P(), P()),
        out_specs=(P("group", "frame", None, None), P("frame", None, "group", None)),
        check_vma=False,
    )
```

```python
import jax
import jax.numpy as jnp
from jax import lax
from jax.experimental import pallas as pl
from jax.sharding import PartitionSpec as P


def shifted(value, axis, steps):
    count = lax.axis_size(axis)
    first, last = (max(0, -steps), min(count, count - steps))
    return lax.ppermute(value, axis, [(source, source + steps) for source in range(first, last)])


def diagonal(value, group_steps, frame_steps):
    groups, frames = lax.axis_size("group"), lax.axis_size("frame")
    pairs = []
    for g in range(groups):
        for f in range(frames):
            h, e = g + group_steps, f + frame_steps
            if 0 <= h < groups and 0 <= e < frames:
                pairs.append((g * frames + f, h * frames + e))
    return lax.ppermute(value, ("group", "frame"), pairs)


def conv3d_kernel(rows_ref, kernel_ref, acc_ref):
    step = pl.program_id(0)
    frames, width, channels = acc_ref.shape[1:]

    @pl.when(step == 0)
    def _():
        acc_ref[...] = jnp.zeros_like(acc_ref)

    lhs = rows_ref[pl.ds(step // 3, frames), step % 3].reshape(frames * width, channels)
    for c in range(3):
        part = jnp.dot(lhs, kernel_ref[0, c], preferred_element_type=jnp.float32)
        acc_ref[c] += part.reshape(frames, width, channels)


def conv3d(rows, kernel3):
    frames, _, width, channels = rows.shape
    count = frames - 2
    taps = kernel3.reshape(9, 3, channels, channels)
    acc = pl.pallas_call(
        conv3d_kernel,
        grid=(9,),
        in_specs=[
            pl.BlockSpec(rows.shape, lambda s: (0, 0, 0, 0)),
            pl.BlockSpec((1, 3, channels, channels), lambda s: (s, 0, 0, 0)),
        ],
        out_specs=pl.BlockSpec((3, count, width, channels), lambda s: (0, 0, 0, 0)),
        out_shape=jax.ShapeDtypeStruct((3, count, width, channels), jnp.float32),
    )(rows, taps)
    zero = jnp.zeros((count, 1, channels), jnp.float32)
    left = jnp.concatenate([zero, acc[0, :, :-1]], axis=1)
    right = jnp.concatenate([acc[2, :, 1:], zero], axis=1)
    return left + acc[1] + right


def shards(video, kernel3, kernel2):
    length, _, width, channels = video.shape
    groups = lax.axis_size("group")
    cached = shifted(video[length - 2 :], "group", 1)
    above = shifted(video, "frame", 1)
    below = shifted(video, "frame", -1)
    cached_above = diagonal(video[length - 2 :], 1, 1)
    cached_below = diagonal(video[length - 2 :], 1, -1)
    rows = jnp.concatenate(
        [
            jnp.concatenate([cached_above, above], 0),
            jnp.concatenate([cached, video], 0),
            jnp.concatenate([cached_below, below], 0),
        ],
        1,
    )
    conv = conv3d(rows, kernel3)
    features = jax.nn.silu(conv).astype(jnp.bfloat16)
    block = width // groups
    padded = jnp.pad(features, ((0, 0), (1, 1), (0, 0)))
    pieces = jnp.stack([padded[:, j * block : j * block + block + 2] for j in range(groups)], 0)
    pieces = lax.all_to_all(pieces, "group", 0, 0, tiled=False)
    pieces = pieces.reshape(groups * length, block + 2, channels)
    rows_all = lax.all_to_all(pieces, "frame", 0, 0, tiled=True)
    critic = lax.conv_general_dilated(
        rows_all[None],
        kernel2,
        (1, 1),
        ((1, 1), (0, 0)),
        dimension_numbers=("NHWC", "HWIO", "NHWC"),
        preferred_element_type=jnp.float32,
    ).astype(jnp.bfloat16)
    return features[:, None], critic


def solution(mesh):
    return jax.shard_map(
        shards,
        mesh=mesh,
        in_specs=(P("group", "frame", None, None), P(), P()),
        out_specs=(P("group", "frame", None, None), P("frame", None, "group", None)),
        check_vma=False,
    )
```

```python
import jax
import jax.numpy as jnp
from jax import lax
from jax.experimental import pallas as pl
from jax.sharding import PartitionSpec as P


def shifted(value, axis, steps):
    count = lax.axis_size(axis)
    first, last = (max(0, -steps), min(count, count - steps))
    return lax.ppermute(value, axis, [(source, source + steps) for source in range(first, last)])


def diagonal(value, group_steps, frame_steps):
    groups, frames = lax.axis_size("group"), lax.axis_size("frame")
    pairs = []
    for g in range(groups):
        for f in range(frames):
            h, e = g + group_steps, f + frame_steps
            if 0 <= h < groups and 0 <= e < frames:
                pairs.append((g * frames + f, h * frames + e))
    return lax.ppermute(value, ("group", "frame"), pairs)


def conv3d_kernel(rows_ref, kernel_ref, *refs):
    acc_ref = refs[-1]
    step = pl.program_id(0)
    pairs = rows_ref.shape[1]
    frames, width, channels = acc_ref.shape[1:]

    if len(refs) == 1:

        @pl.when(step == 0)
        def _():
            acc_ref[...] = jnp.zeros_like(acc_ref)

    else:

        @pl.when(step == 0)
        def _():
            acc_ref[...] = refs[0][...]

    lhs = rows_ref[pl.ds(step // pairs, frames), step % pairs].reshape(frames * width, channels)
    for c in range(3):
        part = jnp.dot(lhs, kernel_ref[0, 0, c], preferred_element_type=jnp.float32)
        acc_ref[c] += part.reshape(frames, width, channels)


def conv3d_taps(rows, kernel3, row_taps, acc=None):
    frames, pairs, width, channels = rows.shape
    count = frames - 2
    if pairs == 1:
        index = lambda s: (s, row_taps[0], 0, 0, 0)
    else:
        index = lambda s: (s // 2, row_taps[0] + (row_taps[1] - row_taps[0]) * (s % 2), 0, 0, 0)
    acc_spec = pl.BlockSpec((3, count, width, channels), lambda s: (0, 0, 0, 0))
    operands = [rows, kernel3] + ([] if acc is None else [acc])
    return pl.pallas_call(
        conv3d_kernel,
        grid=(3 * pairs,),
        in_specs=[
            pl.BlockSpec(rows.shape, lambda s: (0, 0, 0, 0)),
            pl.BlockSpec((1, 1, 3, channels, channels), index),
        ]
        + ([] if acc is None else [acc_spec]),
        out_specs=acc_spec,
        out_shape=jax.ShapeDtypeStruct((3, count, width, channels), jnp.float32),
        input_output_aliases={} if acc is None else {2: 0},
    )(*operands)


def column_sum(acc):
    count, _, channels = acc.shape[1:]
    zero = jnp.zeros((count, 1, channels), jnp.float32)
    left = jnp.concatenate([zero, acc[0, :, :-1]], axis=1)
    right = jnp.concatenate([acc[2, :, 1:], zero], axis=1)
    return left + acc[1] + right


def critic_kernel(cols_ref, kernel_ref, out_ref):
    width = out_ref.shape[1]
    rows, channels = cols_ref.shape[1:]
    total = None
    for c in range(3):
        lhs = cols_ref[c : c + width].reshape(width * rows, channels)
        part = jnp.dot(lhs, kernel_ref[0, c], preferred_element_type=jnp.float32)
        total = part if total is None else total + part
    out_ref[0] = total.reshape(width, rows, channels)


def critic_conv(cols, kernel2):
    span, rows, channels = cols.shape
    width = span - 2
    acc = pl.pallas_call(
        critic_kernel,
        grid=(3,),
        in_specs=[
            pl.BlockSpec(cols.shape, lambda s: (0, 0, 0)),
            pl.BlockSpec((1, 3, channels, channels), lambda s: (s, 0, 0, 0)),
        ],
        out_specs=pl.BlockSpec((1, width, rows, channels), lambda s: (s, 0, 0, 0)),
        out_shape=jax.ShapeDtypeStruct((3, width, rows, channels), jnp.float32),
    )(cols, kernel2)
    zero = jnp.zeros((width, 1, channels), jnp.float32)
    above = jnp.concatenate([zero, acc[0, :, :-1]], axis=1)
    below = jnp.concatenate([acc[2, :, 1:], zero], axis=1)
    total = above + acc[1] + below
    return jnp.transpose(total, (1, 0, 2)).astype(jnp.bfloat16)


def shards(video, kernel3, kernel2):
    length, _, width, channels = video.shape
    groups = lax.axis_size("group")
    cached = shifted(video[length - 2 :], "group", 1)
    above = shifted(video, "frame", 1)
    below = shifted(video, "frame", -1)
    cached_above = diagonal(video[length - 2 :], 1, 1)
    cached_below = diagonal(video[length - 2 :], 1, -1)
    centre = jnp.concatenate([cached, video], 0)
    acc = conv3d_taps(centre, kernel3, (1,))
    edges = jnp.concatenate(
        [jnp.concatenate([cached_above, above], 0), jnp.concatenate([cached_below, below], 0)], 1
    )
    acc = conv3d_taps(edges, kernel3, (0, 2), acc)
    features = jax.nn.silu(column_sum(acc)).astype(jnp.bfloat16)
    block = width // groups
    padded = jnp.pad(features, ((0, 0), (1, 1), (0, 0)))
    pieces = jnp.stack([padded[:, j * block : j * block + block + 2] for j in range(groups)], 0)
    pieces = lax.all_to_all(pieces, "group", 0, 0, tiled=False)
    pieces = pieces.reshape(groups * length, block + 2, channels)
    cols = lax.all_to_all(pieces, "frame", 0, 1, tiled=False)
    critic = critic_conv(cols, kernel2)
    return features[:, None], critic[None]


def solution(mesh):
    return jax.shard_map(
        shards,
        mesh=mesh,
        in_specs=(P("group", "frame", None, None), P(), P()),
        out_specs=(P("group", "frame", None, None), P("frame", None, "group", None)),
        check_vma=False,
    )
```

```python
import jax
import jax.numpy as jnp
from jax import lax
from jax.experimental import pallas as pl
from jax.experimental.pallas import tpu as pltpu
from jax.sharding import PartitionSpec as P


def shifted(value, axis, steps):
    count = lax.axis_size(axis)
    first, last = (max(0, -steps), min(count, count - steps))
    return lax.ppermute(value, axis, [(source, source + steps) for source in range(first, last)])


def diagonal(value, group_steps, frame_steps):
    groups, frames = lax.axis_size("group"), lax.axis_size("frame")
    pairs = []
    for g in range(groups):
        for f in range(frames):
            h, e = g + group_steps, f + frame_steps
            if 0 <= h < groups and 0 <= e < frames:
                pairs.append((g * frames + f, h * frames + e))
    return lax.ppermute(value, ("group", "frame"), pairs)


def shifted_columns(rows):
    width = rows.shape[-2]
    pad = [(0, 0)] * (rows.ndim - 2) + [(1, 1), (0, 0)]
    padded = jnp.pad(rows, pad)
    return jnp.concatenate([padded[..., c : c + width, :] for c in range(3)], axis=-1)


def conv3d_kernel(rows_ref, kernel_ref, *refs):
    out_ref, acc_ref = refs[-2], refs[-1]
    step = pl.program_id(0)
    last = pl.num_programs(0) - 1
    pairs = rows_ref.shape[1]
    frames, width, channels = out_ref.shape
    lhs = rows_ref[pl.ds(step // pairs, frames), step % pairs].reshape(frames * width, 3 * channels)
    part = jnp.dot(lhs, kernel_ref[0, 0], preferred_element_type=jnp.float32).reshape(out_ref.shape)
    if len(refs) == 2:

        @pl.when(step == 0)
        def _():
            acc_ref[...] = part

        @pl.when(step > 0)
        def _():
            acc_ref[...] += part

        @pl.when(step == last)
        def _():
            out_ref[...] = acc_ref[...]

    else:
        prior_ref = refs[0]

        @pl.when(step == 0)
        def _():
            acc_ref[...] = prior_ref[...] + part

        @pl.when(step > 0)
        def _():
            acc_ref[...] += part

        @pl.when(step == last)
        def _():
            out_ref[...] = jax.nn.silu(acc_ref[...]).astype(out_ref.dtype)


def conv3d_taps(rows, kernel3, row_taps, prior=None):
    frames, pairs, width, wide = rows.shape
    channels = wide // 3
    count = frames - 2
    taps = kernel3.reshape(3, 3, 1, wide, channels)
    if pairs == 1:
        index = lambda s: (s, row_taps[0], 0, 0, 0)
    else:
        index = lambda s: (s // 2, row_taps[0] + (row_taps[1] - row_taps[0]) * (s % 2), 0, 0, 0)
    block = (count, width, channels)
    full = pl.BlockSpec(block, lambda s: (0, 0, 0))
    dtype = jnp.float32 if prior is None else jnp.bfloat16
    operands = [rows, taps] + ([] if prior is None else [prior])
    return pl.pallas_call(
        conv3d_kernel,
        grid=(3 * pairs,),
        in_specs=[
            pl.BlockSpec(rows.shape, lambda s: (0, 0, 0, 0)),
            pl.BlockSpec((1, 1, 1, wide, channels), index),
        ]
        + ([] if prior is None else [full]),
        out_specs=full,
        out_shape=jax.ShapeDtypeStruct(block, dtype),
        scratch_shapes=[pltpu.VMEM(block, jnp.float32)],
    )(*operands)


def critic_kernel(lhs_ref, kernel_ref, out_ref):
    rows, width, channels = out_ref.shape
    lhs = lhs_ref[...].reshape(rows * width, lhs_ref.shape[-1])
    total = jnp.dot(lhs, kernel_ref[...], preferred_element_type=jnp.float32)
    out_ref[...] = total.reshape(out_ref.shape).astype(out_ref.dtype)


def critic_conv(features, kernel2):
    rows, span, channels = features.shape
    width = span - 2
    padded = jnp.pad(features, ((1, 1), (0, 0), (0, 0)))
    lhs = jnp.concatenate(
        [padded[b : b + rows, c : c + width] for b in range(3) for c in range(3)], axis=-1
    )
    return pl.pallas_call(
        critic_kernel,
        out_shape=jax.ShapeDtypeStruct((rows, width, channels), jnp.bfloat16),
    )(lhs, kernel2.reshape(9 * channels, channels))


def shards(video, kernel3, kernel2):
    length, _, width, channels = video.shape
    groups = lax.axis_size("group")
    cached = shifted(video[length - 2 :], "group", 1)
    above = shifted(video, "frame", 1)
    below = shifted(video, "frame", -1)
    cached_above = diagonal(video[length - 2 :], 1, 1)
    cached_below = diagonal(video[length - 2 :], 1, -1)
    centre = shifted_columns(jnp.concatenate([cached, video], 0))
    acc = conv3d_taps(centre, kernel3, (1,))
    edges = jnp.concatenate(
        [jnp.concatenate([cached_above, above], 0), jnp.concatenate([cached_below, below], 0)], 1
    )
    features = conv3d_taps(shifted_columns(edges), kernel3, (0, 2), acc)
    block = width // groups
    padded = jnp.pad(features, ((0, 0), (1, 1), (0, 0)))
    pieces = jnp.stack([padded[:, j * block : j * block + block + 2] for j in range(groups)], 0)
    pieces = lax.all_to_all(pieces, "group", 0, 0, tiled=False)
    pieces = pieces.reshape(groups * length, block + 2, channels)
    rows_all = lax.all_to_all(pieces, "frame", 0, 0, tiled=True)
    critic = critic_conv(rows_all, kernel2)
    return features[:, None], critic[None]


def solution(mesh):
    return jax.shard_map(
        shards,
        mesh=mesh,
        in_specs=(P("group", "frame", None, None), P(), P()),
        out_specs=(P("group", "frame", None, None), P("frame", None, "group", None)),
        check_vma=False,
    )
```

```python
import jax
import jax.numpy as jnp
from jax import lax
from jax.experimental import pallas as pl
from jax.experimental.pallas import tpu as pltpu
from jax.sharding import PartitionSpec as P


def shifted(value, axis, steps):
    count = lax.axis_size(axis)
    first, last = (max(0, -steps), min(count, count - steps))
    return lax.ppermute(value, axis, [(source, source + steps) for source in range(first, last)])


def diagonal(value, group_steps, frame_steps):
    groups, frames = lax.axis_size("group"), lax.axis_size("frame")
    pairs = []
    for g in range(groups):
        for f in range(frames):
            h, e = g + group_steps, f + frame_steps
            if 0 <= h < groups and 0 <= e < frames:
                pairs.append((g * frames + f, h * frames + e))
    return lax.ppermute(value, ("group", "frame"), pairs)


def conv3d_kernel(rows_ref, kernel_ref, *refs):
    out_ref, acc_ref = refs[-2], refs[-1]
    step = pl.program_id(0)
    pairs = rows_ref.shape[1]
    frames, width, channels = acc_ref.shape[1:]

    @pl.when(step == 0)
    def _():
        if len(refs) == 2:
            acc_ref[...] = jnp.zeros_like(acc_ref)
        else:
            acc_ref[...] = refs[0][...]

    lhs = rows_ref[pl.ds(step // pairs, frames), step % pairs].reshape(frames * width, channels)
    for c in range(3):
        part = jnp.dot(lhs, kernel_ref[0, 0, c], preferred_element_type=jnp.float32)
        acc_ref[c] += part.reshape(frames, width, channels)

    @pl.when(step == pl.num_programs(0) - 1)
    def _():
        if len(refs) == 2:
            out_ref[...] = acc_ref[...]
        else:
            column = lax.broadcasted_iota(jnp.int32, (frames, width, channels), 1)
            left = jnp.where(column == 0, 0.0, pltpu.roll(acc_ref[0], 1, 1))
            right = jnp.where(column == width - 1, 0.0, pltpu.roll(acc_ref[2], width - 1, 1))
            total = left + acc_ref[1] + right
            out_ref[...] = (total / (1.0 + jnp.exp(-total))).astype(out_ref.dtype)


def conv3d_taps(rows, kernel3, row_taps, acc=None):
    frames, pairs, width, channels = rows.shape
    count = frames - 2
    if pairs == 1:
        index = lambda s: (s, row_taps[0], 0, 0, 0)
    else:
        index = lambda s: (s // 2, row_taps[0] + (row_taps[1] - row_taps[0]) * (s % 2), 0, 0, 0)
    acc_block = (3, count, width, channels)
    acc_spec = pl.BlockSpec(acc_block, lambda s: (0, 0, 0, 0))
    if acc is None:
        out_spec, out_shape = acc_spec, jax.ShapeDtypeStruct(acc_block, jnp.float32)
    else:
        out_spec = pl.BlockSpec((count, width, channels), lambda s: (0, 0, 0))
        out_shape = jax.ShapeDtypeStruct((count, width, channels), jnp.bfloat16)
    operands = [rows, kernel3] + ([] if acc is None else [acc])
    return pl.pallas_call(
        conv3d_kernel,
        grid=(3 * pairs,),
        in_specs=[
            pl.BlockSpec(rows.shape, lambda s: (0, 0, 0, 0)),
            pl.BlockSpec((1, 1, 3, channels, channels), index),
        ]
        + ([] if acc is None else [acc_spec]),
        out_specs=out_spec,
        out_shape=out_shape,
        scratch_shapes=[pltpu.VMEM(acc_block, jnp.float32)],
    )(*operands)


def shards(video, kernel3, kernel2):
    length, _, width, channels = video.shape
    groups = lax.axis_size("group")
    cached = shifted(video[length - 2 :], "group", 1)
    above = shifted(video, "frame", 1)
    below = shifted(video, "frame", -1)
    cached_above = diagonal(video[length - 2 :], 1, 1)
    cached_below = diagonal(video[length - 2 :], 1, -1)
    centre = jnp.concatenate([cached, video], 0)
    acc = conv3d_taps(centre, kernel3, (1,))
    edges = jnp.concatenate(
        [jnp.concatenate([cached_above, above], 0), jnp.concatenate([cached_below, below], 0)], 1
    )
    features = conv3d_taps(edges, kernel3, (0, 2), acc)
    block = width // groups
    padded = jnp.pad(features, ((0, 0), (1, 1), (0, 0)))
    pieces = jnp.stack([padded[:, j * block : j * block + block + 2] for j in range(groups)], 0)
    pieces = lax.all_to_all(pieces, "group", 0, 0, tiled=False)
    pieces = pieces.reshape(groups * length, block + 2, channels)
    rows_all = lax.all_to_all(pieces, "frame", 0, 0, tiled=True)
    critic = lax.conv_general_dilated(
        rows_all[None],
        kernel2,
        (1, 1),
        ((1, 1), (0, 0)),
        dimension_numbers=("NHWC", "HWIO", "NHWC"),
        preferred_element_type=jnp.float32,
    ).astype(jnp.bfloat16)
    return features[:, None], critic


def solution(mesh):
    return jax.shard_map(
        shards,
        mesh=mesh,
        in_specs=(P("group", "frame", None, None), P(), P()),
        out_specs=(P("group", "frame", None, None), P("frame", None, "group", None)),
        check_vma=False,
    )
```

```python
import jax
import jax.numpy as jnp
from jax import lax
from jax.experimental import pallas as pl
from jax.sharding import PartitionSpec as P


def shifted(value, axis, steps):
    count = lax.axis_size(axis)
    first, last = (max(0, -steps), min(count, count - steps))
    return lax.ppermute(value, axis, [(source, source + steps) for source in range(first, last)])


def diagonal(value, group_steps, frame_steps):
    groups, frames = lax.axis_size("group"), lax.axis_size("frame")
    pairs = []
    for g in range(groups):
        for f in range(frames):
            h, e = g + group_steps, f + frame_steps
            if 0 <= h < groups and 0 <= e < frames:
                pairs.append((g * frames + f, h * frames + e))
    return lax.ppermute(value, ("group", "frame"), pairs)


def conv3d_kernel(rows_ref, kernel_ref, *refs):
    acc_ref = refs[-1]
    step = pl.program_id(0)
    pairs = rows_ref.shape[1]
    frames, width, channels = acc_ref.shape[1:]

    if len(refs) == 1:

        @pl.when(step == 0)
        def _():
            acc_ref[...] = jnp.zeros_like(acc_ref)

    else:

        @pl.when(step == 0)
        def _():
            acc_ref[...] = refs[0][...]

    lhs = rows_ref[pl.ds(step // pairs, frames), step % pairs].reshape(frames * width, channels)
    for c in range(3):
        part = jnp.dot(lhs, kernel_ref[0, 0, c], preferred_element_type=jnp.float32)
        acc_ref[c] += part.reshape(frames, width, channels)


def conv3d_taps(rows, kernel3, row_taps, acc=None):
    frames, pairs, width, channels = rows.shape
    count = frames - 2
    if pairs == 1:
        index = lambda s: (s, row_taps[0], 0, 0, 0)
    else:
        index = lambda s: (s // 2, row_taps[0] + (row_taps[1] - row_taps[0]) * (s % 2), 0, 0, 0)
    acc_spec = pl.BlockSpec((3, count, width, channels), lambda s: (0, 0, 0, 0))
    operands = [rows, kernel3] + ([] if acc is None else [acc])
    return pl.pallas_call(
        conv3d_kernel,
        grid=(3 * pairs,),
        in_specs=[
            pl.BlockSpec(rows.shape, lambda s: (0, 0, 0, 0)),
            pl.BlockSpec((1, 1, 3, channels, channels), index),
        ]
        + ([] if acc is None else [acc_spec]),
        out_specs=acc_spec,
        out_shape=jax.ShapeDtypeStruct((3, count, width, channels), jnp.float32),
        input_output_aliases={} if acc is None else {2: 0},
    )(*operands)


def column_sum(acc):
    count, _, channels = acc.shape[1:]
    zero = jnp.zeros((count, 1, channels), jnp.float32)
    left = jnp.concatenate([zero, acc[0, :, :-1]], axis=1)
    right = jnp.concatenate([acc[2, :, 1:], zero], axis=1)
    return left + acc[1] + right


def shards(video, kernel3, kernel2):
    length, _, width, channels = video.shape
    groups = lax.axis_size("group")
    cached = shifted(video[length - 2 :], "group", 1)
    above = shifted(video, "frame", 1)
    below = shifted(video, "frame", -1)
    cached_above = diagonal(video[length - 2 :], 1, 1)
    cached_below = diagonal(video[length - 2 :], 1, -1)
    centre = jnp.concatenate([cached, video], 0)
    acc = conv3d_taps(centre, kernel3, (1,))
    edges = jnp.concatenate(
        [jnp.concatenate([cached_above, above], 0), jnp.concatenate([cached_below, below], 0)], 1
    )
    acc = conv3d_taps(edges, kernel3, (0, 2), acc)
    features = jax.nn.silu(column_sum(acc)).astype(jnp.bfloat16)
    block = width // groups
    padded = jnp.pad(features, ((0, 0), (1, 1), (0, 0)))
    pieces = jnp.stack([padded[:, j * block : j * block + block + 2] for j in range(groups)], 0)
    pieces = lax.all_to_all(pieces, "group", 0, 0, tiled=False)
    pieces = pieces.reshape(groups * length, block + 2, channels)
    rows_all = lax.all_to_all(pieces, "frame", 0, 0, tiled=True)
    critic = lax.conv_general_dilated(
        rows_all[None],
        kernel2,
        (1, 1),
        ((1, 1), (0, 0)),
        dimension_numbers=("NHWC", "HWIO", "NHWC"),
        preferred_element_type=jnp.float32,
    ).astype(jnp.bfloat16)
    return features[:, None], critic


def solution(mesh):
    return jax.shard_map(
        shards,
        mesh=mesh,
        in_specs=(P("group", "frame", None, None), P(), P()),
        out_specs=(P("group", "frame", None, None), P("frame", None, "group", None)),
        check_vma=False,
    )
```

```python
import jax
import jax.numpy as jnp
from jax import lax
from jax.experimental import pallas as pl
from jax.experimental.pallas import tpu as pltpu
from jax.sharding import PartitionSpec as P


def shifted(value, axis, steps):
    count = lax.axis_size(axis)
    first, last = (max(0, -steps), min(count, count - steps))
    return lax.ppermute(value, axis, [(source, source + steps) for source in range(first, last)])


def diagonal(value, group_steps, frame_steps):
    groups, frames = lax.axis_size("group"), lax.axis_size("frame")
    pairs = []
    for g in range(groups):
        for f in range(frames):
            h, e = g + group_steps, f + frame_steps
            if 0 <= h < groups and 0 <= e < frames:
                pairs.append((g * frames + f, h * frames + e))
    return lax.ppermute(value, ("group", "frame"), pairs)


def conv3d_kernel(rows_ref, kernel_ref, *refs):
    acc_ref = refs[-1]
    step = pl.program_id(0)
    pairs = rows_ref.shape[1]
    frames, width, channels = acc_ref.shape[1:]

    if len(refs) == 1:

        @pl.when(step == 0)
        def _():
            acc_ref[...] = jnp.zeros_like(acc_ref)

    else:

        @pl.when(step == 0)
        def _():
            acc_ref[...] = refs[0][...]

    lhs = rows_ref[pl.ds(step // pairs, frames), step % pairs].reshape(frames * width, channels)
    for c in range(3):
        part = jnp.dot(lhs, kernel_ref[0, 0, c], preferred_element_type=jnp.float32)
        acc_ref[c] += part.reshape(frames, width, channels)


def conv3d_taps(rows, kernel3, row_taps, acc=None):
    frames, pairs, width, channels = rows.shape
    count = frames - 2
    if pairs == 1:
        index = lambda s: (s, row_taps[0], 0, 0, 0)
    else:
        index = lambda s: (s // 2, row_taps[0] + (row_taps[1] - row_taps[0]) * (s % 2), 0, 0, 0)
    acc_spec = pl.BlockSpec((3, count, width, channels), lambda s: (0, 0, 0, 0))
    operands = [rows, kernel3] + ([] if acc is None else [acc])
    return pl.pallas_call(
        conv3d_kernel,
        grid=(3 * pairs,),
        in_specs=[
            pl.BlockSpec(rows.shape, lambda s: (0, 0, 0, 0)),
            pl.BlockSpec((1, 1, 3, channels, channels), index),
        ]
        + ([] if acc is None else [acc_spec]),
        out_specs=acc_spec,
        out_shape=jax.ShapeDtypeStruct((3, count, width, channels), jnp.float32),
        input_output_aliases={} if acc is None else {2: 0},
    )(*operands)


def column_sum(acc):
    count, _, channels = acc.shape[1:]
    zero = jnp.zeros((count, 1, channels), jnp.float32)
    left = jnp.concatenate([zero, acc[0, :, :-1]], axis=1)
    right = jnp.concatenate([acc[2, :, 1:], zero], axis=1)
    return left + acc[1] + right


def row_partials_kernel(rows_ref, kernel_ref, out_ref, acc_ref):
    step = pl.program_id(0)
    tap = step % 3
    frames, width, channels = out_ref.shape[1:]

    @pl.when(tap == 0)
    def _():
        acc_ref[...] = jnp.zeros_like(acc_ref)

    lhs = rows_ref[pl.ds(tap, frames), 0].reshape(frames * width, channels)
    for c in range(3):
        part = jnp.dot(lhs, kernel_ref[0, 0, c], preferred_element_type=jnp.float32)
        acc_ref[c] += part.reshape(frames, width, channels)

    @pl.when(tap == 2)
    def _():
        column = lax.broadcasted_iota(jnp.int32, (frames, width, channels), 1)
        left = jnp.where(column == 0, 0.0, pltpu.roll(acc_ref[0], 1, 1))
        right = jnp.where(column == width - 1, 0.0, pltpu.roll(acc_ref[2], width - 1, 1))
        out_ref[0] = left + acc_ref[1] + right


def row_partials(rows, kernel3):
    frames, _, width, channels = rows.shape
    count = frames - 2
    return pl.pallas_call(
        row_partials_kernel,
        grid=(9,),
        in_specs=[
            pl.BlockSpec(rows.shape, lambda s: (0, 0, 0, 0)),
            pl.BlockSpec((1, 1, 3, channels, channels), lambda s: (s % 3, s // 3, 0, 0, 0)),
        ],
        out_specs=pl.BlockSpec((1, count, width, channels), lambda s: (s // 3, 0, 0, 0)),
        out_shape=jax.ShapeDtypeStruct((3, count, width, channels), jnp.float32),
        scratch_shapes=[pltpu.VMEM((3, count, width, channels), jnp.float32)],
    )(rows, kernel3)


def shards(video, kernel3, kernel2):
    length, _, width, channels = video.shape
    groups = lax.axis_size("group")
    cached = shifted(video[length - 2 :], "group", 1)
    partials = row_partials(jnp.concatenate([cached, video], 0), kernel3)
    from_above = shifted(partials[0].astype(jnp.bfloat16), "frame", 1)
    from_below = shifted(partials[2].astype(jnp.bfloat16), "frame", -1)
    conv = partials[1] + from_above.astype(jnp.float32) + from_below.astype(jnp.float32)
    features = jax.nn.silu(conv).astype(jnp.bfloat16)
    block = width // groups
    padded = jnp.pad(features, ((0, 0), (1, 1), (0, 0)))
    pieces = jnp.stack([padded[:, j * block : j * block + block + 2] for j in range(groups)], 0)
    pieces = lax.all_to_all(pieces, "group", 0, 0, tiled=False)
    pieces = pieces.reshape(groups * length, block + 2, channels)
    rows_all = lax.all_to_all(pieces, "frame", 0, 0, tiled=True)
    critic = lax.conv_general_dilated(
        rows_all[None],
        kernel2,
        (1, 1),
        ((1, 1), (0, 0)),
        dimension_numbers=("NHWC", "HWIO", "NHWC"),
        preferred_element_type=jnp.float32,
    ).astype(jnp.bfloat16)
    return features[:, None], critic


def solution(mesh):
    return jax.shard_map(
        shards,
        mesh=mesh,
        in_specs=(P("group", "frame", None, None), P(), P()),
        out_specs=(P("group", "frame", None, None), P("frame", None, "group", None)),
        check_vma=False,
    )
```

```python
import jax
import jax.numpy as jnp
from jax import lax
from jax.experimental import pallas as pl
from jax.experimental.pallas import tpu as pltpu
from jax.sharding import PartitionSpec as P


def shifted(value, axis, steps):
    count = lax.axis_size(axis)
    first, last = (max(0, -steps), min(count, count - steps))
    return lax.ppermute(value, axis, [(source, source + steps) for source in range(first, last)])


def diagonal(value, group_steps, frame_steps):
    groups, frames = lax.axis_size("group"), lax.axis_size("frame")
    pairs = []
    for g in range(groups):
        for f in range(frames):
            h, e = g + group_steps, f + frame_steps
            if 0 <= h < groups and 0 <= e < frames:
                pairs.append((g * frames + f, h * frames + e))
    return lax.ppermute(value, ("group", "frame"), pairs)


def conv3d_kernel(rows_ref, kernel_ref, *refs):
    acc_ref = refs[-1]
    step = pl.program_id(0)
    pairs = rows_ref.shape[1]
    frames, width, channels = acc_ref.shape[1:]

    if len(refs) == 1:

        @pl.when(step == 0)
        def _():
            acc_ref[...] = jnp.zeros_like(acc_ref)

    else:

        @pl.when(step == 0)
        def _():
            acc_ref[...] = refs[0][...]

    lhs = rows_ref[pl.ds(step // pairs, frames), step % pairs].reshape(frames * width, channels)
    for c in range(3):
        part = jnp.dot(lhs, kernel_ref[0, 0, c], preferred_element_type=jnp.float32)
        acc_ref[c] += part.reshape(frames, width, channels)


def conv3d_taps(rows, kernel3, row_taps, acc=None):
    frames, pairs, width, channels = rows.shape
    count = frames - 2
    if pairs == 1:
        index = lambda s: (s, row_taps[0], 0, 0, 0)
    else:
        index = lambda s: (s // 2, row_taps[0] + (row_taps[1] - row_taps[0]) * (s % 2), 0, 0, 0)
    acc_spec = pl.BlockSpec((3, count, width, channels), lambda s: (0, 0, 0, 0))
    operands = [rows, kernel3] + ([] if acc is None else [acc])
    return pl.pallas_call(
        conv3d_kernel,
        grid=(3 * pairs,),
        in_specs=[
            pl.BlockSpec(rows.shape, lambda s: (0, 0, 0, 0)),
            pl.BlockSpec((1, 1, 3, channels, channels), index),
        ]
        + ([] if acc is None else [acc_spec]),
        out_specs=acc_spec,
        out_shape=jax.ShapeDtypeStruct((3, count, width, channels), jnp.float32),
        input_output_aliases={} if acc is None else {2: 0},
    )(*operands)


def column_sum(acc):
    count, _, channels = acc.shape[1:]
    zero = jnp.zeros((count, 1, channels), jnp.float32)
    left = jnp.concatenate([zero, acc[0, :, :-1]], axis=1)
    right = jnp.concatenate([acc[2, :, 1:], zero], axis=1)
    return left + acc[1] + right


def row_partials_kernel(rows_ref, kernel_ref, out_ref, acc_ref):
    step = pl.program_id(0)
    tap = step % 3
    frames, width, channels = out_ref.shape[1:]

    @pl.when(tap == 0)
    def _():
        acc_ref[...] = jnp.zeros_like(acc_ref)

    lhs = rows_ref[pl.ds(tap, frames), 0].reshape(frames * width, channels)
    for c in range(3):
        part = jnp.dot(lhs, kernel_ref[0, 0, c], preferred_element_type=jnp.float32)
        acc_ref[c] += part.reshape(frames, width, channels)

    @pl.when(tap == 2)
    def _():
        column = lax.broadcasted_iota(jnp.int32, (frames, width, channels), 1)
        left = jnp.where(column == 0, 0.0, pltpu.roll(acc_ref[0], 1, 1))
        right = jnp.where(column == width - 1, 0.0, pltpu.roll(acc_ref[2], width - 1, 1))
        out_ref[0] = left + acc_ref[1] + right


def row_partials(rows, kernel3, row_taps):
    frames, _, width, channels = rows.shape
    count = frames - 2
    first, stride = row_taps[0], (row_taps[-1] - row_taps[0]) if len(row_taps) > 1 else 0
    return pl.pallas_call(
        row_partials_kernel,
        grid=(3 * len(row_taps),),
        in_specs=[
            pl.BlockSpec(rows.shape, lambda s: (0, 0, 0, 0)),
            pl.BlockSpec((1, 1, 3, channels, channels), lambda s: (s % 3, first + stride * (s // 3), 0, 0, 0)),
        ],
        out_specs=pl.BlockSpec((1, count, width, channels), lambda s: (s // 3, 0, 0, 0)),
        out_shape=jax.ShapeDtypeStruct((len(row_taps), count, width, channels), jnp.float32),
        scratch_shapes=[pltpu.VMEM((3, count, width, channels), jnp.float32)],
    )(rows, kernel3)


def shards(video, kernel3, kernel2):
    length, _, width, channels = video.shape
    groups = lax.axis_size("group")
    cached = shifted(video[length - 2 :], "group", 1)
    rows = jnp.concatenate([cached, video], 0)
    edges = row_partials(rows, kernel3, (0, 2))
    from_above = shifted(edges[0].astype(jnp.bfloat16), "frame", 1)
    from_below = shifted(edges[1].astype(jnp.bfloat16), "frame", -1)
    centre = row_partials(rows, kernel3, (1,))[0]
    conv = centre + from_above.astype(jnp.float32) + from_below.astype(jnp.float32)
    features = jax.nn.silu(conv).astype(jnp.bfloat16)
    block = width // groups
    padded = jnp.pad(features, ((0, 0), (1, 1), (0, 0)))
    pieces = jnp.stack([padded[:, j * block : j * block + block + 2] for j in range(groups)], 0)
    pieces = lax.all_to_all(pieces, "group", 0, 0, tiled=False)
    pieces = pieces.reshape(groups * length, block + 2, channels)
    rows_all = lax.all_to_all(pieces, "frame", 0, 0, tiled=True)
    critic = lax.conv_general_dilated(
        rows_all[None],
        kernel2,
        (1, 1),
        ((1, 1), (0, 0)),
        dimension_numbers=("NHWC", "HWIO", "NHWC"),
        preferred_element_type=jnp.float32,
    ).astype(jnp.bfloat16)
    return features[:, None], critic


def solution(mesh):
    return jax.shard_map(
        shards,
        mesh=mesh,
        in_specs=(P("group", "frame", None, None), P(), P()),
        out_specs=(P("group", "frame", None, None), P("frame", None, "group", None)),
        check_vma=False,
    )
```

```python
import functools

import jax
import jax.numpy as jnp
from jax import lax
from jax.experimental import pallas as pl
from jax.experimental.pallas import tpu as pltpu
from jax.sharding import PartitionSpec as P


def shifted(value, axis, steps):
    count = lax.axis_size(axis)
    first, last = (max(0, -steps), min(count, count - steps))
    return lax.ppermute(value, axis, [(source, source + steps) for source in range(first, last)])


def diagonal(value, group_steps, frame_steps):
    groups, frames = lax.axis_size("group"), lax.axis_size("frame")
    pairs = []
    for g in range(groups):
        for f in range(frames):
            h, e = g + group_steps, f + frame_steps
            if 0 <= h < groups and 0 <= e < frames:
                pairs.append((g * frames + f, h * frames + e))
    return lax.ppermute(value, ("group", "frame"), pairs)


def conv3d_kernel(*refs, pairs, final):
    sources, kernel_ref = refs[: 2 * pairs], refs[2 * pairs]
    out_ref, acc_ref, rows_ref = refs[-3:]
    step = pl.program_id(0)
    frames, width, channels = acc_ref.shape[1:]
    cached = sources[0].shape[0]

    @pl.when(step == 0)
    def _():
        for p in range(pairs):
            rows_ref[p, :cached] = sources[2 * p][:, 0]
            rows_ref[p, cached:] = sources[2 * p + 1][:, 0]
        if final:
            acc_ref[...] = refs[2 * pairs + 1][...]
        else:
            acc_ref[...] = jnp.zeros_like(acc_ref)

    lhs = rows_ref[step % pairs, pl.ds(step // pairs, frames)].reshape(frames * width, channels)
    for c in range(3):
        part = jnp.dot(lhs, kernel_ref[0, 0, c], preferred_element_type=jnp.float32)
        acc_ref[c] += part.reshape(frames, width, channels)

    @pl.when(step == pl.num_programs(0) - 1)
    def _():
        if final:
            column = lax.broadcasted_iota(jnp.int32, (frames, width, channels), 1)
            left = jnp.where(column == 0, 0.0, pltpu.roll(acc_ref[0], 1, 1))
            right = jnp.where(column == width - 1, 0.0, pltpu.roll(acc_ref[2], width - 1, 1))
            out_ref[...] = left + acc_ref[1] + right
        else:
            out_ref[...] = acc_ref[...]


def conv3d_taps(sources, kernel3, row_taps, acc=None):
    pairs = len(row_taps)
    cached, _, width, channels = sources[0].shape
    count = sources[1].shape[0]
    if pairs == 1:
        index = lambda s: (s, row_taps[0], 0, 0, 0)
    else:
        index = lambda s: (s // 2, row_taps[0] + (row_taps[1] - row_taps[0]) * (s % 2), 0, 0, 0)
    acc_block = (3, count, width, channels)
    acc_spec = pl.BlockSpec(acc_block, lambda s: (0, 0, 0, 0))
    if acc is None:
        out_spec, out_block = acc_spec, acc_block
    else:
        out_spec, out_block = pl.BlockSpec(acc_block[1:], lambda s: (0, 0, 0)), acc_block[1:]
    whole = lambda x: pl.BlockSpec(x.shape, lambda s: (0,) * x.ndim)
    return pl.pallas_call(
        functools.partial(conv3d_kernel, pairs=pairs, final=acc is not None),
        grid=(3 * pairs,),
        in_specs=[whole(x) for x in sources]
        + [pl.BlockSpec((1, 1, 3, channels, channels), index)]
        + ([] if acc is None else [acc_spec]),
        out_specs=out_spec,
        out_shape=jax.ShapeDtypeStruct(out_block, jnp.float32),
        scratch_shapes=[
            pltpu.VMEM(acc_block, jnp.float32),
            pltpu.VMEM((pairs, cached + count, width, channels), sources[0].dtype),
        ],
    )(*sources, kernel3, *([] if acc is None else [acc]))


def shards(video, kernel3, kernel2):
    length, _, width, channels = video.shape
    groups = lax.axis_size("group")
    cached = shifted(video[length - 2 :], "group", 1)
    above = shifted(video, "frame", 1)
    below = shifted(video, "frame", -1)
    cached_above = diagonal(video[length - 2 :], 1, 1)
    cached_below = diagonal(video[length - 2 :], 1, -1)
    acc = conv3d_taps((cached, video), kernel3, (1,))
    conv = conv3d_taps((cached_above, above, cached_below, below), kernel3, (0, 2), acc)
    features = jax.nn.silu(conv).astype(jnp.bfloat16)
    block = width // groups
    padded = jnp.pad(features, ((0, 0), (1, 1), (0, 0)))
    pieces = jnp.stack([padded[:, j * block : j * block + block + 2] for j in range(groups)], 0)
    pieces = lax.all_to_all(pieces, "group", 0, 0, tiled=False)
    pieces = pieces.reshape(groups * length, block + 2, channels)
    rows_all = lax.all_to_all(pieces, "frame", 0, 0, tiled=True)
    critic = lax.conv_general_dilated(
        rows_all[None],
        kernel2,
        (1, 1),
        ((1, 1), (0, 0)),
        dimension_numbers=("NHWC", "HWIO", "NHWC"),
        preferred_element_type=jnp.float32,
    ).astype(jnp.bfloat16)
    return features[:, None], critic


def solution(mesh):
    return jax.shard_map(
        shards,
        mesh=mesh,
        in_specs=(P("group", "frame", None, None), P(), P()),
        out_specs=(P("group", "frame", None, None), P("frame", None, "group", None)),
        check_vma=False,
    )
```

```python
import jax
import jax.numpy as jnp
from jax import lax
from jax.experimental import pallas as pl
from jax.sharding import PartitionSpec as P


def shifted(value, axis, steps):
    count = lax.axis_size(axis)
    first, last = (max(0, -steps), min(count, count - steps))
    return lax.ppermute(value, axis, [(source, source + steps) for source in range(first, last)])


def diagonal(value, group_steps, frame_steps):
    groups, frames = lax.axis_size("group"), lax.axis_size("frame")
    pairs = []
    for g in range(groups):
        for f in range(frames):
            h, e = g + group_steps, f + frame_steps
            if 0 <= h < groups and 0 <= e < frames:
                pairs.append((g * frames + f, h * frames + e))
    return lax.ppermute(value, ("group", "frame"), pairs)


def conv3d_kernel(rows_ref, kernel_ref, *refs):
    acc_ref = refs[-1]
    step = pl.program_id(0)
    pairs = rows_ref.shape[1]
    frames, width, channels = acc_ref.shape[1:]

    if len(refs) == 1:

        @pl.when(step == 0)
        def _():
            acc_ref[...] = jnp.zeros_like(acc_ref)

    else:

        @pl.when(step == 0)
        def _():
            acc_ref[...] = refs[0][...]

    lhs = rows_ref[pl.ds(step // pairs, frames), step % pairs].reshape(frames * width, channels)
    for c in range(3):
        part = jnp.dot(lhs, kernel_ref[0, 0, c], preferred_element_type=jnp.float32)
        acc_ref[c] += part.reshape(frames, width, channels)


def conv3d_taps(rows, kernel3, row_taps, acc=None):
    frames, pairs, width, channels = rows.shape
    count = frames - 2
    if pairs == 1:
        index = lambda s: (s, row_taps[0], 0, 0, 0)
    else:
        index = lambda s: (s // 2, row_taps[0] + (row_taps[1] - row_taps[0]) * (s % 2), 0, 0, 0)
    acc_spec = pl.BlockSpec((3, count, width, channels), lambda s: (0, 0, 0, 0))
    operands = [rows, kernel3] + ([] if acc is None else [acc])
    return pl.pallas_call(
        conv3d_kernel,
        grid=(3 * pairs,),
        in_specs=[
            pl.BlockSpec(rows.shape, lambda s: (0, 0, 0, 0)),
            pl.BlockSpec((1, 1, 3, channels, channels), index),
        ]
        + ([] if acc is None else [acc_spec]),
        out_specs=acc_spec,
        out_shape=jax.ShapeDtypeStruct((3, count, width, channels), jnp.float32),
        input_output_aliases={} if acc is None else {2: 0},
    )(*operands)


def column_sum(acc):
    count, _, channels = acc.shape[1:]
    zero = jnp.zeros((count, 1, channels), jnp.float32)
    left = jnp.concatenate([zero, acc[0, :, :-1]], axis=1)
    right = jnp.concatenate([acc[2, :, 1:], zero], axis=1)
    return left + acc[1] + right


def shards(video, kernel3, kernel2):
    length, _, width, channels = video.shape
    groups = lax.axis_size("group")
    cached = shifted(video[length - 2 :], "group", 1)
    above = shifted(video, "frame", 1)
    below = shifted(video, "frame", -1)
    cached_above = diagonal(video[length - 2 :], 1, 1)
    cached_below = diagonal(video[length - 2 :], 1, -1)
    centre = jnp.concatenate([cached, video], 0)
    acc = conv3d_taps(centre, kernel3, (1,))
    edges = jnp.concatenate(
        [jnp.concatenate([cached_above, above], 0), jnp.concatenate([cached_below, below], 0)], 1
    )
    acc = conv3d_taps(edges, kernel3, (0, 2), acc)
    features = jax.nn.silu(column_sum(acc)).astype(jnp.bfloat16)
    block = width // groups
    padded = jnp.pad(features, ((0, 0), (1, 1), (0, 0)))
    pieces = jnp.stack([padded[:, j * block : j * block + block + 2] for j in range(groups)], 0)
    pieces = lax.all_to_all(pieces, "group", 0, 0, tiled=False)
    pieces = pieces.reshape(groups * length, block + 2, channels)
    rows_all = lax.all_to_all(pieces, "frame", 0, 0, tiled=True)
    rows, span = rows_all.shape[:2]
    padded = jnp.pad(rows_all, ((1, 1), (0, 0), (0, 0)))
    lhs = jnp.concatenate(
        [padded[b : b + rows, c : c + span - 2] for b in range(3) for c in range(3)], axis=-1
    )
    critic = jnp.dot(
        lhs.reshape(rows * (span - 2), 9 * channels),
        kernel2.reshape(9 * channels, channels),
        preferred_element_type=jnp.float32,
    )
    critic = critic.reshape(1, rows, span - 2, channels).astype(jnp.bfloat16)
    return features[:, None], critic


def solution(mesh):
    return jax.shard_map(
        shards,
        mesh=mesh,
        in_specs=(P("group", "frame", None, None), P(), P()),
        out_specs=(P("group", "frame", None, None), P("frame", None, "group", None)),
        check_vma=False,
    )
```

```python
import jax
import jax.numpy as jnp
from jax import lax
from jax.experimental import pallas as pl
from jax.sharding import PartitionSpec as P


def shifted(value, axis, steps):
    count = lax.axis_size(axis)
    first, last = (max(0, -steps), min(count, count - steps))
    return lax.ppermute(value, axis, [(source, source + steps) for source in range(first, last)])


def diagonal(value, group_steps, frame_steps):
    groups, frames = lax.axis_size("group"), lax.axis_size("frame")
    pairs = []
    for g in range(groups):
        for f in range(frames):
            h, e = g + group_steps, f + frame_steps
            if 0 <= h < groups and 0 <= e < frames:
                pairs.append((g * frames + f, h * frames + e))
    return lax.ppermute(value, ("group", "frame"), pairs)


def conv3d_kernel(rows_ref, kernel_ref, *refs):
    acc_ref = refs[-1]
    step = pl.program_id(0)
    pairs = rows_ref.shape[1]
    frames, width, channels = acc_ref.shape[1:]

    if len(refs) == 1:

        @pl.when(step == 0)
        def _():
            acc_ref[...] = jnp.zeros_like(acc_ref)

    else:

        @pl.when(step == 0)
        def _():
            acc_ref[...] = refs[0][...]

    lhs = rows_ref[pl.ds(step // pairs, frames), step % pairs].reshape(frames * width, channels)
    for c in range(3):
        part = jnp.dot(lhs, kernel_ref[0, 0, c], preferred_element_type=jnp.float32)
        acc_ref[c] += part.reshape(frames, width, channels)


def conv3d_taps(rows, kernel3, row_taps, acc=None):
    frames, pairs, width, channels = rows.shape
    count = frames - 2
    if pairs == 1:
        index = lambda s: (s, row_taps[0], 0, 0, 0)
    else:
        index = lambda s: (s // 2, row_taps[0] + (row_taps[1] - row_taps[0]) * (s % 2), 0, 0, 0)
    acc_spec = pl.BlockSpec((3, count, width, channels), lambda s: (0, 0, 0, 0))
    operands = [rows, kernel3] + ([] if acc is None else [acc])
    return pl.pallas_call(
        conv3d_kernel,
        grid=(3 * pairs,),
        in_specs=[
            pl.BlockSpec(rows.shape, lambda s: (0, 0, 0, 0)),
            pl.BlockSpec((1, 1, 3, channels, channels), index),
        ]
        + ([] if acc is None else [acc_spec]),
        out_specs=acc_spec,
        out_shape=jax.ShapeDtypeStruct((3, count, width, channels), jnp.float32),
        input_output_aliases={} if acc is None else {2: 0},
    )(*operands)


def column_sum(acc):
    count, _, channels = acc.shape[1:]
    zero = jnp.zeros((count, 1, channels), jnp.float32)
    left = jnp.concatenate([zero, acc[0, :, :-1]], axis=1)
    right = jnp.concatenate([acc[2, :, 1:], zero], axis=1)
    return left + acc[1] + right


def shards(video, kernel3, kernel2):
    length, _, width, channels = video.shape
    groups = lax.axis_size("group")
    cached = shifted(video[length - 2 :], "group", 1)
    above = shifted(video, "frame", 1)
    below = shifted(video, "frame", -1)
    cached_above = diagonal(video[length - 2 :], 1, 1)
    cached_below = diagonal(video[length - 2 :], 1, -1)
    rows = jnp.concatenate(
        [
            jnp.concatenate([cached_above, above], 0),
            jnp.concatenate([cached, video], 0),
            jnp.concatenate([cached_below, below], 0),
        ],
        1,
    )
    padded = jnp.pad(rows, ((0, 0), (0, 0), (1, 1), (0, 0)))
    lhs = jnp.concatenate(
        [padded[a : a + length, b, c : c + width] for a in range(3) for b in range(3) for c in range(3)], axis=-1
    )
    conv = jnp.dot(
        lhs.reshape(length * width, 27 * channels),
        kernel3.reshape(27 * channels, channels),
        preferred_element_type=jnp.float32,
    )
    features = jax.nn.silu(conv.reshape(length, width, channels)).astype(jnp.bfloat16)
    block = width // groups
    padded = jnp.pad(features, ((0, 0), (1, 1), (0, 0)))
    pieces = jnp.stack([padded[:, j * block : j * block + block + 2] for j in range(groups)], 0)
    pieces = lax.all_to_all(pieces, "group", 0, 0, tiled=False)
    pieces = pieces.reshape(groups * length, block + 2, channels)
    rows_all = lax.all_to_all(pieces, "frame", 0, 0, tiled=True)
    rows, span = rows_all.shape[:2]
    padded = jnp.pad(rows_all, ((1, 1), (0, 0), (0, 0)))
    lhs = jnp.concatenate(
        [padded[b : b + rows, c : c + span - 2] for b in range(3) for c in range(3)], axis=-1
    )
    critic = jnp.dot(
        lhs.reshape(rows * (span - 2), 9 * channels),
        kernel2.reshape(9 * channels, channels),
        preferred_element_type=jnp.float32,
    )
    critic = critic.reshape(1, rows, span - 2, channels).astype(jnp.bfloat16)
    return features[:, None], critic


def solution(mesh):
    return jax.shard_map(
        shards,
        mesh=mesh,
        in_specs=(P("group", "frame", None, None), P(), P()),
        out_specs=(P("group", "frame", None, None), P("frame", None, "group", None)),
        check_vma=False,
    )
```

```python
import jax
import jax.numpy as jnp
from jax import lax
from jax.experimental import pallas as pl
from jax.sharding import PartitionSpec as P


def shifted(value, axis, steps):
    count = lax.axis_size(axis)
    first, last = (max(0, -steps), min(count, count - steps))
    return lax.ppermute(value, axis, [(source, source + steps) for source in range(first, last)])


def diagonal(value, group_steps, frame_steps):
    groups, frames = lax.axis_size("group"), lax.axis_size("frame")
    pairs = []
    for g in range(groups):
        for f in range(frames):
            h, e = g + group_steps, f + frame_steps
            if 0 <= h < groups and 0 <= e < frames:
                pairs.append((g * frames + f, h * frames + e))
    return lax.ppermute(value, ("group", "frame"), pairs)


def conv3d_kernel(rows_ref, kernel_ref, *refs):
    acc_ref = refs[-1]
    step = pl.program_id(0)
    pairs = rows_ref.shape[1]
    frames, width, channels = acc_ref.shape[1:]

    if len(refs) == 1:

        @pl.when(step == 0)
        def _():
            acc_ref[...] = jnp.zeros_like(acc_ref)

    else:

        @pl.when(step == 0)
        def _():
            acc_ref[...] = refs[0][...]

    lhs = rows_ref[pl.ds(step // pairs, frames), step % pairs].reshape(frames * width, channels)
    for c in range(3):
        part = jnp.dot(lhs, kernel_ref[0, 0, c], preferred_element_type=jnp.float32)
        acc_ref[c] += part.reshape(frames, width, channels)


def conv3d_taps(rows, kernel3, row_taps, acc=None):
    frames, pairs, width, channels = rows.shape
    count = frames - 2
    if pairs == 1:
        index = lambda s: (s, row_taps[0], 0, 0, 0)
    else:
        index = lambda s: (s // 2, row_taps[0] + (row_taps[1] - row_taps[0]) * (s % 2), 0, 0, 0)
    acc_spec = pl.BlockSpec((3, count, width, channels), lambda s: (0, 0, 0, 0))
    operands = [rows, kernel3] + ([] if acc is None else [acc])
    return pl.pallas_call(
        conv3d_kernel,
        grid=(3 * pairs,),
        in_specs=[
            pl.BlockSpec(rows.shape, lambda s: (0, 0, 0, 0)),
            pl.BlockSpec((1, 1, 3, channels, channels), index),
        ]
        + ([] if acc is None else [acc_spec]),
        out_specs=acc_spec,
        out_shape=jax.ShapeDtypeStruct((3, count, width, channels), jnp.float32),
        input_output_aliases={} if acc is None else {2: 0},
    )(*operands)


def column_sum(acc):
    count, _, channels = acc.shape[1:]
    zero = jnp.zeros((count, 1, channels), jnp.float32)
    left = jnp.concatenate([zero, acc[0, :, :-1]], axis=1)
    right = jnp.concatenate([acc[2, :, 1:], zero], axis=1)
    return left + acc[1] + right


def shards(video, kernel3, kernel2):
    length, _, width, channels = video.shape
    groups = lax.axis_size("group")
    cached = shifted(video[length - 2 :], "group", 1)
    above = shifted(video, "frame", 1)
    below = shifted(video, "frame", -1)
    cached_above = diagonal(video[length - 2 :], 1, 1)
    cached_below = diagonal(video[length - 2 :], 1, -1)
    rows = jnp.concatenate(
        [
            jnp.concatenate([cached_above, above], 0),
            jnp.concatenate([cached, video], 0),
            jnp.concatenate([cached_below, below], 0),
        ],
        1,
    )
    padded = jnp.pad(rows, ((0, 0), (0, 0), (1, 1), (0, 0)))
    conv = None
    for a in range(3):
        lhs = jnp.concatenate(
            [padded[a : a + length, b, c : c + width] for b in range(3) for c in range(3)], axis=-1
        )
        part = jnp.dot(
            lhs.reshape(length * width, 9 * channels),
            kernel3[a].reshape(9 * channels, channels),
            preferred_element_type=jnp.float32,
        )
        conv = part if conv is None else conv + part
    features = jax.nn.silu(conv.reshape(length, width, channels)).astype(jnp.bfloat16)
    block = width // groups
    padded = jnp.pad(features, ((0, 0), (1, 1), (0, 0)))
    pieces = jnp.stack([padded[:, j * block : j * block + block + 2] for j in range(groups)], 0)
    pieces = lax.all_to_all(pieces, "group", 0, 0, tiled=False)
    pieces = pieces.reshape(groups * length, block + 2, channels)
    rows_all = lax.all_to_all(pieces, "frame", 0, 0, tiled=True)
    rows, span = rows_all.shape[:2]
    padded = jnp.pad(rows_all, ((1, 1), (0, 0), (0, 0)))
    lhs = jnp.concatenate(
        [padded[b : b + rows, c : c + span - 2] for b in range(3) for c in range(3)], axis=-1
    )
    critic = jnp.dot(
        lhs.reshape(rows * (span - 2), 9 * channels),
        kernel2.reshape(9 * channels, channels),
        preferred_element_type=jnp.float32,
    )
    critic = critic.reshape(1, rows, span - 2, channels).astype(jnp.bfloat16)
    return features[:, None], critic


def solution(mesh):
    return jax.shard_map(
        shards,
        mesh=mesh,
        in_specs=(P("group", "frame", None, None), P(), P()),
        out_specs=(P("group", "frame", None, None), P("frame", None, "group", None)),
        check_vma=False,
    )
```

```python
import jax
import jax.numpy as jnp
from jax import lax
from jax.experimental import pallas as pl
from jax.sharding import PartitionSpec as P


def shifted(value, axis, steps):
    count = lax.axis_size(axis)
    first, last = (max(0, -steps), min(count, count - steps))
    return lax.ppermute(value, axis, [(source, source + steps) for source in range(first, last)])


def diagonal(value, group_steps, frame_steps):
    groups, frames = lax.axis_size("group"), lax.axis_size("frame")
    pairs = []
    for g in range(groups):
        for f in range(frames):
            h, e = g + group_steps, f + frame_steps
            if 0 <= h < groups and 0 <= e < frames:
                pairs.append((g * frames + f, h * frames + e))
    return lax.ppermute(value, ("group", "frame"), pairs)


def conv3d_kernel(rows_ref, kernel_ref, *refs):
    acc_ref = refs[-1]
    step = pl.program_id(0)
    pairs = rows_ref.shape[1]
    frames, width, channels = acc_ref.shape[1:]

    if len(refs) == 1:

        @pl.when(step == 0)
        def _():
            acc_ref[...] = jnp.zeros_like(acc_ref)

    else:

        @pl.when(step == 0)
        def _():
            acc_ref[...] = refs[0][...]

    lhs = rows_ref[pl.ds(step // pairs, frames), step % pairs].reshape(frames * width, channels)
    for c in range(3):
        part = jnp.dot(lhs, kernel_ref[0, 0, c], preferred_element_type=jnp.float32)
        acc_ref[c] += part.reshape(frames, width, channels)


def conv3d_taps(rows, kernel3, row_taps, acc=None):
    frames, pairs, width, channels = rows.shape
    count = frames - 2
    if pairs == 1:
        index = lambda s: (s, row_taps[0], 0, 0, 0)
    else:
        index = lambda s: (s // 2, row_taps[0] + (row_taps[1] - row_taps[0]) * (s % 2), 0, 0, 0)
    acc_spec = pl.BlockSpec((3, count, width, channels), lambda s: (0, 0, 0, 0))
    operands = [rows, kernel3] + ([] if acc is None else [acc])
    return pl.pallas_call(
        conv3d_kernel,
        grid=(3 * pairs,),
        in_specs=[
            pl.BlockSpec(rows.shape, lambda s: (0, 0, 0, 0)),
            pl.BlockSpec((1, 1, 3, channels, channels), index),
        ]
        + ([] if acc is None else [acc_spec]),
        out_specs=acc_spec,
        out_shape=jax.ShapeDtypeStruct((3, count, width, channels), jnp.float32),
        input_output_aliases={} if acc is None else {2: 0},
    )(*operands)


def column_sum(acc):
    count, _, channels = acc.shape[1:]
    zero = jnp.zeros((count, 1, channels), jnp.float32)
    left = jnp.concatenate([zero, acc[0, :, :-1]], axis=1)
    right = jnp.concatenate([acc[2, :, 1:], zero], axis=1)
    return left + acc[1] + right


def shards(video, kernel3, kernel2):
    length, _, width, channels = video.shape
    groups = lax.axis_size("group")
    cached = shifted(video[length - 2 :], "group", 1)
    above = shifted(video, "frame", 1)
    below = shifted(video, "frame", -1)
    cached_above = diagonal(video[length - 2 :], 1, 1)
    cached_below = diagonal(video[length - 2 :], 1, -1)
    rows = jnp.concatenate(
        [
            jnp.concatenate([cached_above, above], 0),
            jnp.concatenate([cached, video], 0),
            jnp.concatenate([cached_below, below], 0),
        ],
        1,
    )
    shifts = [
        jnp.pad(rows[:, :, : width - 1], ((0, 0), (0, 0), (1, 0), (0, 0))),
        rows,
        jnp.pad(rows[:, :, 1:], ((0, 0), (0, 0), (0, 1), (0, 0))),
    ]
    lhs = jnp.concatenate(
        [shifts[c][a : a + length, b] for a in range(3) for b in range(3) for c in range(3)], axis=-1
    )
    conv = jnp.dot(
        lhs.reshape(length * width, 27 * channels),
        kernel3.reshape(27 * channels, channels),
        preferred_element_type=jnp.float32,
    )
    features = jax.nn.silu(conv.reshape(length, width, channels)).astype(jnp.bfloat16)
    block = width // groups
    padded = jnp.pad(features, ((0, 0), (1, 1), (0, 0)))
    pieces = jnp.stack([padded[:, j * block : j * block + block + 2] for j in range(groups)], 0)
    pieces = lax.all_to_all(pieces, "group", 0, 0, tiled=False)
    pieces = pieces.reshape(groups * length, block + 2, channels)
    rows_all = lax.all_to_all(pieces, "frame", 0, 0, tiled=True)
    rows, span = rows_all.shape[:2]
    padded = jnp.pad(rows_all, ((1, 1), (0, 0), (0, 0)))
    lhs = jnp.concatenate(
        [padded[b : b + rows, c : c + span - 2] for b in range(3) for c in range(3)], axis=-1
    )
    critic = jnp.dot(
        lhs.reshape(rows * (span - 2), 9 * channels),
        kernel2.reshape(9 * channels, channels),
        preferred_element_type=jnp.float32,
    )
    critic = critic.reshape(1, rows, span - 2, channels).astype(jnp.bfloat16)
    return features[:, None], critic


def solution(mesh):
    return jax.shard_map(
        shards,
        mesh=mesh,
        in_specs=(P("group", "frame", None, None), P(), P()),
        out_specs=(P("group", "frame", None, None), P("frame", None, "group", None)),
        check_vma=False,
    )
```

```python
import jax
import jax.numpy as jnp
from jax import lax
from jax.experimental import pallas as pl
from jax.sharding import PartitionSpec as P


def shifted(value, axis, steps):
    count = lax.axis_size(axis)
    first, last = (max(0, -steps), min(count, count - steps))
    return lax.ppermute(value, axis, [(source, source + steps) for source in range(first, last)])


def diagonal(value, group_steps, frame_steps):
    groups, frames = lax.axis_size("group"), lax.axis_size("frame")
    pairs = []
    for g in range(groups):
        for f in range(frames):
            h, e = g + group_steps, f + frame_steps
            if 0 <= h < groups and 0 <= e < frames:
                pairs.append((g * frames + f, h * frames + e))
    return lax.ppermute(value, ("group", "frame"), pairs)


def conv3d_kernel(rows_ref, kernel_ref, *refs):
    acc_ref = refs[-1]
    step = pl.program_id(0)
    pairs = rows_ref.shape[1]
    frames, width, channels = acc_ref.shape[1:]

    if len(refs) == 1:

        @pl.when(step == 0)
        def _():
            acc_ref[...] = jnp.zeros_like(acc_ref)

    else:

        @pl.when(step == 0)
        def _():
            acc_ref[...] = refs[0][...]

    lhs = rows_ref[pl.ds(step // pairs, frames), step % pairs].reshape(frames * width, channels)
    for c in range(3):
        part = jnp.dot(lhs, kernel_ref[0, 0, c], preferred_element_type=jnp.float32)
        acc_ref[c] += part.reshape(frames, width, channels)


def conv3d_taps(rows, kernel3, row_taps, acc=None):
    frames, pairs, width, channels = rows.shape
    count = frames - 2
    if pairs == 1:
        index = lambda s: (s, row_taps[0], 0, 0, 0)
    else:
        index = lambda s: (s // 2, row_taps[0] + (row_taps[1] - row_taps[0]) * (s % 2), 0, 0, 0)
    acc_spec = pl.BlockSpec((3, count, width, channels), lambda s: (0, 0, 0, 0))
    operands = [rows, kernel3] + ([] if acc is None else [acc])
    return pl.pallas_call(
        conv3d_kernel,
        grid=(3 * pairs,),
        in_specs=[
            pl.BlockSpec(rows.shape, lambda s: (0, 0, 0, 0)),
            pl.BlockSpec((1, 1, 3, channels, channels), index),
        ]
        + ([] if acc is None else [acc_spec]),
        out_specs=acc_spec,
        out_shape=jax.ShapeDtypeStruct((3, count, width, channels), jnp.float32),
        input_output_aliases={} if acc is None else {2: 0},
    )(*operands)


def column_sum(acc):
    count, _, channels = acc.shape[1:]
    zero = jnp.zeros((count, 1, channels), jnp.float32)
    left = jnp.concatenate([zero, acc[0, :, :-1]], axis=1)
    right = jnp.concatenate([acc[2, :, 1:], zero], axis=1)
    return left + acc[1] + right


def shards(video, kernel3, kernel2):
    length, _, width, channels = video.shape
    groups = lax.axis_size("group")
    cached = shifted(video[length - 2 :], "group", 1)
    above = shifted(video, "frame", 1)
    below = shifted(video, "frame", -1)
    cached_above = diagonal(video[length - 2 :], 1, 1)
    cached_below = diagonal(video[length - 2 :], 1, -1)
    rows = jnp.concatenate(
        [
            jnp.concatenate([cached_above, above], 0),
            jnp.concatenate([cached, video], 0),
            jnp.concatenate([cached_below, below], 0),
        ],
        1,
    )
    padded = jnp.pad(rows, ((0, 0), (0, 0), (1, 1), (0, 0)))
    lhs = jnp.concatenate(
        [padded[a : a + length, b, c : c + width] for a in range(3) for b in range(3) for c in range(3)], axis=-1
    )
    conv = jnp.dot(
        lhs.reshape(length * width, 27 * channels),
        kernel3.reshape(27 * channels, channels),
        preferred_element_type=jnp.float32,
    )
    features = jax.nn.silu(conv.reshape(length, width, channels)).astype(jnp.bfloat16)
    block = width // groups
    padded = jnp.pad(features, ((0, 0), (1, 1), (0, 0)))
    pieces = jnp.stack([padded[:, j * block : j * block + block + 2] for j in range(groups)], 0)
    pieces = lax.all_to_all(pieces, "group", 0, 0, tiled=False)
    pieces = pieces.reshape(groups * length, block + 2, channels)
    rows_all = lax.all_to_all(pieces, "frame", 0, 0, tiled=True)
    rows, span = rows_all.shape[:2]
    shifts = [
        jnp.pad(rows_all[: rows - 1], ((1, 0), (0, 0), (0, 0))),
        rows_all,
        jnp.pad(rows_all[1:], ((0, 1), (0, 0), (0, 0))),
    ]
    lhs = jnp.concatenate(
        [shifts[b][:, c : c + span - 2] for b in range(3) for c in range(3)], axis=-1
    )
    critic = jnp.dot(
        lhs.reshape(rows * (span - 2), 9 * channels),
        kernel2.reshape(9 * channels, channels),
        preferred_element_type=jnp.float32,
    )
    critic = critic.reshape(1, rows, span - 2, channels).astype(jnp.bfloat16)
    return features[:, None], critic


def solution(mesh):
    return jax.shard_map(
        shards,
        mesh=mesh,
        in_specs=(P("group", "frame", None, None), P(), P()),
        out_specs=(P("group", "frame", None, None), P("frame", None, "group", None)),
        check_vma=False,
    )
```

```python
import jax
import jax.numpy as jnp
from jax import lax
from jax.experimental import pallas as pl
from jax.sharding import PartitionSpec as P


def shifted(value, axis, steps):
    count = lax.axis_size(axis)
    first, last = (max(0, -steps), min(count, count - steps))
    return lax.ppermute(value, axis, [(source, source + steps) for source in range(first, last)])


def diagonal(value, group_steps, frame_steps):
    groups, frames = lax.axis_size("group"), lax.axis_size("frame")
    pairs = []
    for g in range(groups):
        for f in range(frames):
            h, e = g + group_steps, f + frame_steps
            if 0 <= h < groups and 0 <= e < frames:
                pairs.append((g * frames + f, h * frames + e))
    return lax.ppermute(value, ("group", "frame"), pairs)


def conv3d_kernel(rows_ref, kernel_ref, *refs):
    acc_ref = refs[-1]
    step = pl.program_id(0)
    pairs = rows_ref.shape[1]
    frames, width, channels = acc_ref.shape[1:]

    if len(refs) == 1:

        @pl.when(step == 0)
        def _():
            acc_ref[...] = jnp.zeros_like(acc_ref)

    else:

        @pl.when(step == 0)
        def _():
            acc_ref[...] = refs[0][...]

    lhs = rows_ref[pl.ds(step // pairs, frames), step % pairs].reshape(frames * width, channels)
    for c in range(3):
        part = jnp.dot(lhs, kernel_ref[0, 0, c], preferred_element_type=jnp.float32)
        acc_ref[c] += part.reshape(frames, width, channels)


def conv3d_taps(rows, kernel3, row_taps, acc=None):
    frames, pairs, width, channels = rows.shape
    count = frames - 2
    if pairs == 1:
        index = lambda s: (s, row_taps[0], 0, 0, 0)
    else:
        index = lambda s: (s // 2, row_taps[0] + (row_taps[1] - row_taps[0]) * (s % 2), 0, 0, 0)
    acc_spec = pl.BlockSpec((3, count, width, channels), lambda s: (0, 0, 0, 0))
    operands = [rows, kernel3] + ([] if acc is None else [acc])
    return pl.pallas_call(
        conv3d_kernel,
        grid=(3 * pairs,),
        in_specs=[
            pl.BlockSpec(rows.shape, lambda s: (0, 0, 0, 0)),
            pl.BlockSpec((1, 1, 3, channels, channels), index),
        ]
        + ([] if acc is None else [acc_spec]),
        out_specs=acc_spec,
        out_shape=jax.ShapeDtypeStruct((3, count, width, channels), jnp.float32),
        input_output_aliases={} if acc is None else {2: 0},
    )(*operands)


def column_sum(acc):
    count, _, channels = acc.shape[1:]
    zero = jnp.zeros((count, 1, channels), jnp.float32)
    left = jnp.concatenate([zero, acc[0, :, :-1]], axis=1)
    right = jnp.concatenate([acc[2, :, 1:], zero], axis=1)
    return left + acc[1] + right


def shards(video, kernel3, kernel2):
    length, _, width, channels = video.shape
    groups = lax.axis_size("group")
    cached = shifted(video, "group", 1)[length - 2 :]
    above = shifted(video, "frame", 1)
    below = shifted(video, "frame", -1)
    cached_above = diagonal(video, 1, 1)[length - 2 :]
    cached_below = diagonal(video, 1, -1)[length - 2 :]
    rows = jnp.concatenate(
        [
            jnp.concatenate([cached_above, above], 0),
            jnp.concatenate([cached, video], 0),
            jnp.concatenate([cached_below, below], 0),
        ],
        1,
    )
    padded = jnp.pad(rows, ((0, 0), (0, 0), (1, 1), (0, 0)))
    lhs = jnp.concatenate(
        [padded[a : a + length, b, c : c + width] for a in range(3) for b in range(3) for c in range(3)], axis=-1
    )
    conv = jnp.dot(
        lhs.reshape(length * width, 27 * channels),
        kernel3.reshape(27 * channels, channels),
        preferred_element_type=jnp.float32,
    )
    features = jax.nn.silu(conv.reshape(length, width, channels)).astype(jnp.bfloat16)
    block = width // groups
    padded = jnp.pad(features, ((0, 0), (1, 1), (0, 0)))
    pieces = jnp.stack([padded[:, j * block : j * block + block + 2] for j in range(groups)], 0)
    pieces = lax.all_to_all(pieces, "group", 0, 0, tiled=False)
    pieces = pieces.reshape(groups * length, block + 2, channels)
    rows_all = lax.all_to_all(pieces, "frame", 0, 0, tiled=True)
    rows, span = rows_all.shape[:2]
    shifts = [
        jnp.pad(rows_all[: rows - 1], ((1, 0), (0, 0), (0, 0))),
        rows_all,
        jnp.pad(rows_all[1:], ((0, 1), (0, 0), (0, 0))),
    ]
    lhs = jnp.concatenate(
        [shifts[b][:, c : c + span - 2] for b in range(3) for c in range(3)], axis=-1
    )
    critic = jnp.dot(
        lhs.reshape(rows * (span - 2), 9 * channels),
        kernel2.reshape(9 * channels, channels),
        preferred_element_type=jnp.float32,
    )
    critic = critic.reshape(1, rows, span - 2, channels).astype(jnp.bfloat16)
    return features[:, None], critic


def solution(mesh):
    return jax.shard_map(
        shards,
        mesh=mesh,
        in_specs=(P("group", "frame", None, None), P(), P()),
        out_specs=(P("group", "frame", None, None), P("frame", None, "group", None)),
        check_vma=False,
    )
```

```python
import jax
import jax.numpy as jnp
from jax import lax
from jax.experimental import pallas as pl
from jax.sharding import PartitionSpec as P


def shifted(value, axis, steps):
    count = lax.axis_size(axis)
    first, last = (max(0, -steps), min(count, count - steps))
    return lax.ppermute(value, axis, [(source, source + steps) for source in range(first, last)])


def diagonal(value, group_steps, frame_steps):
    groups, frames = lax.axis_size("group"), lax.axis_size("frame")
    pairs = []
    for g in range(groups):
        for f in range(frames):
            h, e = g + group_steps, f + frame_steps
            if 0 <= h < groups and 0 <= e < frames:
                pairs.append((g * frames + f, h * frames + e))
    return lax.ppermute(value, ("group", "frame"), pairs)


def conv3d_kernel(rows_ref, kernel_ref, *refs):
    acc_ref = refs[-1]
    step = pl.program_id(0)
    pairs = rows_ref.shape[1]
    frames, width, channels = acc_ref.shape[1:]

    if len(refs) == 1:

        @pl.when(step == 0)
        def _():
            acc_ref[...] = jnp.zeros_like(acc_ref)

    else:

        @pl.when(step == 0)
        def _():
            acc_ref[...] = refs[0][...]

    lhs = rows_ref[pl.ds(step // pairs, frames), step % pairs].reshape(frames * width, channels)
    for c in range(3):
        part = jnp.dot(lhs, kernel_ref[0, 0, c], preferred_element_type=jnp.float32)
        acc_ref[c] += part.reshape(frames, width, channels)


def conv3d_taps(rows, kernel3, row_taps, acc=None):
    frames, pairs, width, channels = rows.shape
    count = frames - 2
    if pairs == 1:
        index = lambda s: (s, row_taps[0], 0, 0, 0)
    else:
        index = lambda s: (s // 2, row_taps[0] + (row_taps[1] - row_taps[0]) * (s % 2), 0, 0, 0)
    acc_spec = pl.BlockSpec((3, count, width, channels), lambda s: (0, 0, 0, 0))
    operands = [rows, kernel3] + ([] if acc is None else [acc])
    return pl.pallas_call(
        conv3d_kernel,
        grid=(3 * pairs,),
        in_specs=[
            pl.BlockSpec(rows.shape, lambda s: (0, 0, 0, 0)),
            pl.BlockSpec((1, 1, 3, channels, channels), index),
        ]
        + ([] if acc is None else [acc_spec]),
        out_specs=acc_spec,
        out_shape=jax.ShapeDtypeStruct((3, count, width, channels), jnp.float32),
        input_output_aliases={} if acc is None else {2: 0},
    )(*operands)


def column_sum(acc):
    count, _, channels = acc.shape[1:]
    zero = jnp.zeros((count, 1, channels), jnp.float32)
    left = jnp.concatenate([zero, acc[0, :, :-1]], axis=1)
    right = jnp.concatenate([acc[2, :, 1:], zero], axis=1)
    return left + acc[1] + right


def shards(video, kernel3, kernel2):
    length, _, width, channels = video.shape
    groups = lax.axis_size("group")
    cached = shifted(video[length - 2 :], "group", 1)
    above = shifted(video, "frame", 1)
    below = shifted(video, "frame", -1)
    cached_above = diagonal(video[length - 2 :], 1, 1)
    cached_below = diagonal(video[length - 2 :], 1, -1)
    rows = jnp.concatenate(
        [
            jnp.concatenate([cached_above, above], 0),
            jnp.concatenate([cached, video], 0),
            jnp.concatenate([cached_below, below], 0),
        ],
        1,
    )
    shifts = [
        jnp.pad(rows[:, :, : width - 1], ((0, 0), (0, 0), (1, 0), (0, 0))),
        rows,
        jnp.pad(rows[:, :, 1:], ((0, 0), (0, 0), (0, 1), (0, 0))),
    ]
    lhs = jnp.concatenate(
        [shifts[c][a : a + length, b] for a in range(3) for b in range(3) for c in range(3)], axis=-1
    )
    conv = jnp.dot(
        lhs.reshape(length * width, 27 * channels),
        kernel3.reshape(27 * channels, channels),
        preferred_element_type=jnp.float32,
    )
    features = jax.nn.silu(conv.reshape(length, width, channels)).astype(jnp.bfloat16)
    block = width // groups
    padded = jnp.pad(features, ((0, 0), (1, 1), (0, 0)))
    pieces = jnp.stack([padded[:, j * block : j * block + block + 2] for j in range(groups)], 0)
    pieces = lax.all_to_all(pieces, "group", 0, 0, tiled=False)
    pieces = pieces.reshape(groups * length, block + 2, channels)
    rows_all = lax.all_to_all(pieces, "frame", 0, 0, tiled=True)
    rows, span = rows_all.shape[:2]
    shifts = [
        jnp.pad(rows_all[: rows - 1], ((1, 0), (0, 0), (0, 0))),
        rows_all,
        jnp.pad(rows_all[1:], ((0, 1), (0, 0), (0, 0))),
    ]
    lhs = jnp.concatenate(
        [shifts[b][:, c : c + span - 2] for b in range(3) for c in range(3)], axis=-1
    )
    critic = jnp.dot(
        lhs.reshape(rows * (span - 2), 9 * channels),
        kernel2.reshape(9 * channels, channels),
        preferred_element_type=jnp.float32,
    )
    critic = critic.reshape(1, rows, span - 2, channels).astype(jnp.bfloat16)
    return features[:, None], critic


def solution(mesh):
    return jax.shard_map(
        shards,
        mesh=mesh,
        in_specs=(P("group", "frame", None, None), P(), P()),
        out_specs=(P("group", "frame", None, None), P("frame", None, "group", None)),
        check_vma=False,
    )
```
